256 devices in a mesh: frame: 32 (over z, x_hi, core), head: 8 (over y, x_lo).
Axes of the slice: x: 4 (x_hi: 2, x_lo: 2; x = x_hi * 2 + x_lo), y: 4, z: 8, core: 2. Of those that a mesh axis runs over, the one named last changes fastest.
Arguments:
- query_vectors: bfloat16 [12288, 3072], P('frame', 'head'), may hold values from -17 to 17
- key_vectors: bfloat16 [12288, 3072], P('frame', 'head'), may hold values from -6 to 6
- value_vectors: bfloat16 [12288, 3072], P('frame', 'head'), may hold values from -6 to 6
- tile_mask: int32 [96, 96], replicated, may hold values from 0 to 1, as said below
- out_weight: bfloat16 [3072, 3072], P('head'), may hold values from -0.109375 to 0.109375
Outputs:
- projected: bfloat16 [12288, 3072], P(('frame', 'head'))
The draws below stay inside these ranges and needn't reach their ends.
Inputs may be any that keep to these rules, and one draw needn't show every extreme that they name: The slab holds packed clips of whole tiles. Each clip lays its tiles out in order on a grid of latent frames by tile rows by tile columns. One clip spans 72 tiles and its latent frame holds 48 tiles, in 4 or 8 columns; every other clip has 2 to 4 rows and 2 to 4 columns, by clip. tile_mask[a, b] is 1 exactly when tiles a and b lie in the same clip and their frame, row and column indices each differ by at most 1.
All inputs are finite; a program needn't handle non-finite values.
Results may differ from the reference program's by a relative error of at most 0.02.
Values may be sent and summed in bfloat16 or wider, within the bound.
No kernel may reach another device: no remote copies, remote signals or barrier semaphores. Data moves between devices by JAX's collectives and lax.ppermute only.
A program may use at most 128 MiB of HBM per device.

```python
import math
import jax
import jax.numpy as jnp
from jax import lax

D = 3072
HEADS = 24
HD = 128
TILE = 128
TOKENS = 12288
NT = 96


def query_key_pair(key):
    channels = HEADS * HD
    query_seed = jax.random.fold_in(key, 11)
    key_seed = jax.random.fold_in(key, 12)
    keys_drawn = jnp.clip(jax.random.normal(key_seed, (TOKENS, channels), jnp.float32), -6.0, 6.0)
    queries_drawn = jnp.clip(jax.random.normal(query_seed, (TOKENS, channels), jnp.float32), -6.0, 6.0)
    return (queries_drawn, keys_drawn)


def draw_query_vectors(key, part):
    return query_key_pair(key)[0].astype(jnp.bfloat16)


def draw_key_vectors(key, part):
    return query_key_pair(key)[1].astype(jnp.bfloat16)


def draw_tile_mask(key, part):
    tile_index = jnp.arange(NT, dtype=jnp.int32)
    big_span = 3 * NT // 4
    offset = jax.random.randint(jax.random.fold_in(key, 21), (), 0, NT - big_span + 1)
    inside = (tile_index > offset) & (tile_index < offset + big_span)
    in_big = (tile_index >= offset) & (tile_index < offset + big_span)
    clip_cuts = jax.random.randint(jax.random.fold_in(key, 22), (NT,), 0, 3) == 0
    clip_cuts = clip_cuts & jnp.logical_not(inside) | (tile_index == offset) | (tile_index == offset + big_span) | (tile_index == 0)
    clip_id = jnp.cumsum(clip_cuts.astype(jnp.int32))
    clip_start = lax.cummax(jnp.where(clip_cuts, tile_index, 0), axis=0)
    big_cols = 4 * (1 + jax.random.randint(jax.random.fold_in(key, 25), (), 0, 2))
    big_rows = NT // (2 * big_cols)
    small_rows = jax.random.randint(jax.random.fold_in(key, 23), (NT + 2,), 2, 5)[clip_id]
    small_cols = jax.random.randint(jax.random.fold_in(key, 24), (NT + 2,), 2, 5)[clip_id]
    grid_rows = jnp.where(in_big, big_rows, small_rows)
    grid_cols = jnp.where(in_big, big_cols, small_cols)
    within = tile_index - clip_start
    col_pos = within % grid_cols
    row_pos = within // grid_cols % grid_rows
    time_pos = within // (grid_cols * grid_rows)
    same_clip = clip_id[:, None] == clip_id[None, :]
    near_time = jnp.abs(time_pos[:, None] - time_pos[None, :]) <= 1
    near_row = jnp.abs(row_pos[:, None] - row_pos[None, :]) <= 1
    near_col = jnp.abs(col_pos[:, None] - col_pos[None, :]) <= 1
    return (same_clip & near_time & near_row & near_col).astype(jnp.int32)


def block_scale(rng, dims, pieces, low, high):
    factor_of, own = 1.0, jax.random.fold_in(rng, 6)
    for dim, blocks in pieces:
        draws = jnp.exp(jax.random.uniform(jax.random.fold_in(own, dim), (blocks,), jnp.float32, low / len(pieces), high / len(pieces)))
        factor_of = factor_of * jnp.repeat(draws, dims[dim] // blocks).reshape([-1 if axis == dim else 1 for axis in range(len(dims))])
    return factor_of


def noise(own_key, shape, deviation, reach, cuts=(), kind=jnp.bfloat16):
    gain = block_scale(own_key, shape, cuts, -0.22, 0.18) if cuts else 1.0
    values = jax.random.normal(own_key, shape, jnp.float32) * deviation * gain
    return jnp.minimum(jnp.maximum(values, -reach), reach).astype(kind)


def setup_inputs(seed: int = 0) -> dict:
    keys = jax.random.split(jax.random.key(seed), 6)
    query_vectors = draw_query_vectors(jax.random.fold_in(keys[5], 71), 0)
    key_vectors = draw_key_vectors(jax.random.fold_in(keys[5], 71), 0)
    value_vectors = noise(keys[2], (TOKENS, D), 1.0, 6.0, ((0, 32), (1, 8)))
    tile_mask = draw_tile_mask(jax.random.fold_in(keys[5], 71), 0)
    out_weight = noise(keys[4], (D, D), D ** -0.5, 0.109375, ((0, 8),))
    return dict(query_vectors=query_vectors, key_vectors=key_vectors, value_vectors=value_vectors, tile_mask=tile_mask, out_weight=out_weight)


def head_rows(query_rows, row_tiles, key_head, value_head, tile_mask):
    raw_scores = jnp.dot(query_rows, key_head.T, preferred_element_type=jnp.float32) * (1.0 / math.sqrt(HD))
    mask_rows = jnp.take(tile_mask, row_tiles, axis=0)
    allowed = jnp.repeat(mask_rows, TILE, axis=1) > 0
    masked = jnp.where(allowed, raw_scores, jnp.float32(-1e+30))
    row_top = lax.optimization_barrier(jnp.max(masked, axis=1, keepdims=True))
    weights = jnp.where(allowed, jnp.exp(masked - row_top), jnp.float32(0.0))
    totals = lax.optimization_barrier(jnp.sum(weights, axis=1, keepdims=True))
    summed = jnp.dot(weights.astype(jnp.bfloat16), value_head, preferred_element_type=jnp.float32)
    return summed / totals

def reference(query_vectors, key_vectors, value_vectors, tile_mask, out_weight):
    block_rows = math.gcd(TOKENS, 1024)
    query_heads = query_vectors.reshape(TOKENS, HEADS, HD).transpose(1, 0, 2)
    key_heads = key_vectors.reshape(TOKENS, HEADS, HD).transpose(1, 0, 2)
    value_heads = value_vectors.reshape(TOKENS, HEADS, HD).transpose(1, 0, 2)
    tile_index = jnp.arange(TOKENS, dtype=jnp.int32) // TILE

    def one_head(element):
        query_head, key_head, value_head = element

        def one_block(block_index):
            first_row = (block_index * block_rows).astype(jnp.int32)
            query_rows = lax.dynamic_slice_in_dim(query_head, first_row, block_rows, 0)
            row_tiles = lax.dynamic_slice_in_dim(tile_index, first_row, block_rows, 0)
            return head_rows(query_rows, row_tiles, key_head, value_head, tile_mask)
        outputs = lax.map(one_block, jnp.arange(TOKENS // block_rows, dtype=jnp.int32))
        return outputs.reshape(TOKENS, HD)
    all_heads = lax.map(one_head, (query_heads, key_heads, value_heads))
    attended = all_heads.transpose(1, 0, 2).reshape(TOKENS, D).astype(jnp.bfloat16)
    return jnp.dot(attended, out_weight, preferred_element_type=jnp.float32).astype(jnp.bfloat16)
```

```python
import functools
import math

import jax
import jax.numpy as jnp
from jax import lax
from jax.experimental import pallas as pl
from jax.experimental.pallas import tpu as pltpu
from jax.sharding import PartitionSpec as P

HD = 128
TILE = 128
MAX_KEYS = 27
KEYS_PER_STEP = 3


def key_lists(tile_rows):
    row_tiles = tile_rows.shape[1]
    allowed = tile_rows > 0
    position = jnp.cumsum(allowed.astype(jnp.int32), axis=1) - 1
    counts = jnp.minimum(jnp.sum(allowed.astype(jnp.int32), axis=1), MAX_KEYS)
    slot = jnp.where(allowed & (position < MAX_KEYS), position, MAX_KEYS)
    tiles = jnp.broadcast_to(jnp.arange(row_tiles, dtype=jnp.int32), tile_rows.shape)
    lists = jnp.zeros((tile_rows.shape[0], MAX_KEYS + 1), jnp.int32)
    lists = jax.vmap(lambda l, s, t: l.at[s].set(t))(lists, slot, tiles)[:, :MAX_KEYS]
    last = jnp.take_along_axis(lists, jnp.maximum(counts - 1, 0)[:, None], axis=1)
    lists = jnp.where(jnp.arange(MAX_KEYS)[None, :] < counts[:, None], lists, last)
    return lists.reshape(-1), counts


def attention_kernel(lists_ref, counts_ref, q_ref, *refs, head_count, scale):
    key_refs = refs[:KEYS_PER_STEP]
    value_refs = refs[KEYS_PER_STEP : 2 * KEYS_PER_STEP]
    o_ref = refs[2 * KEYS_PER_STEP]
    top_ref, total_ref, acc_ref = refs[2 * KEYS_PER_STEP + 1 :]
    tile = pl.program_id(0)
    step = pl.program_id(1)

    @pl.when(step == 0)
    def _():
        top_ref[...] = jnp.full(top_ref.shape, -jnp.inf, jnp.float32)
        total_ref[...] = jnp.zeros(total_ref.shape, jnp.float32)
        acc_ref[...] = jnp.zeros(acc_ref.shape, jnp.float32)

    for j in range(KEYS_PER_STEP):

        @pl.when(step * KEYS_PER_STEP + j < counts_ref[tile])
        def _():
            for h in range(head_count):
                cols = pl.ds(h * HD, HD)
                q = q_ref[:, cols]
                k = key_refs[j][:, cols]
                s = lax.dot_general(
                    q, k, (((1,), (1,)), ((), ())), preferred_element_type=jnp.float32
                ) * scale
                old_top = top_ref[h]
                new_top = jnp.maximum(old_top, jnp.max(s, axis=1, keepdims=True))
                weights = jnp.exp(s - new_top)
                factor = jnp.exp(old_top - new_top)
                total_ref[h] = total_ref[h] * factor + jnp.sum(weights, axis=1, keepdims=True)
                acc_ref[h] = acc_ref[h] * factor + jnp.dot(
                    weights.astype(jnp.bfloat16),
                    value_refs[j][:, cols],
                    preferred_element_type=jnp.float32,
                )
                top_ref[h] = new_top

    @pl.when(step == pl.num_programs(1) - 1)
    def _():
        for h in range(head_count):
            o_ref[:, pl.ds(h * HD, HD)] = (acc_ref[h] / total_ref[h]).astype(o_ref.dtype)


def sparse_attention(query_vectors, key_piece, value_piece, lists, counts):
    row_count, channels = query_vectors.shape
    head_count = channels // HD
    query_tiles = row_count // TILE
    steps = MAX_KEYS // KEYS_PER_STEP

    def key_spec(j):
        return pl.BlockSpec(
            (TILE, channels),
            lambda i, s, lists_ref, counts_ref: (lists_ref[i * MAX_KEYS + s * KEYS_PER_STEP + j], 0),
        )

    row_spec = pl.BlockSpec((TILE, channels), lambda i, s, lists_ref, counts_ref: (i, 0))
    kernel = functools.partial(
        attention_kernel, head_count=head_count, scale=1.0 / math.sqrt(HD)
    )
    return pl.pallas_call(
        kernel,
        grid_spec=pltpu.PrefetchScalarGridSpec(
            num_scalar_prefetch=2,
            grid=(query_tiles, steps),
            in_specs=[row_spec]
            + [key_spec(j) for j in range(KEYS_PER_STEP)]
            + [key_spec(j) for j in range(KEYS_PER_STEP)],
            out_specs=row_spec,
            scratch_shapes=[
                pltpu.VMEM((head_count, TILE, 1), jnp.float32),
                pltpu.VMEM((head_count, TILE, 1), jnp.float32),
                pltpu.VMEM((head_count, TILE, HD), jnp.float32),
            ],
        ),
        out_shape=jax.ShapeDtypeStruct((row_count, channels), jnp.bfloat16),
        compiler_params=pltpu.CompilerParams(dimension_semantics=("arbitrary", "arbitrary")),
    )(lists, counts, query_vectors, *([key_piece] * KEYS_PER_STEP), *([value_piece] * KEYS_PER_STEP))


def shards(query_vectors, key_vectors, value_vectors, tile_mask, out_weight):
    row_count = query_vectors.shape[0]
    frame_pos = lax.axis_index("frame")
    tiles_here = row_count // TILE
    query_tiles = lax.dynamic_slice_in_dim(tile_mask, frame_pos * tiles_here, tiles_here, 0)
    lists, counts = key_lists(query_tiles)
    key_piece = lax.all_gather(key_vectors, "frame", axis=0, tiled=True)
    value_piece = lax.all_gather(value_vectors, "frame", axis=0, tiled=True)
    attended = sparse_attention(query_vectors, key_piece, value_piece, lists, counts)
    return lax.psum_scatter(
        jnp.dot(attended, out_weight, preferred_element_type=jnp.float32).astype(jnp.bfloat16),
        "head",
        scatter_dimension=0,
        tiled=True,
    )


def solution(mesh):
    in_specs = (P("frame", "head"), P("frame", "head"), P("frame", "head"), P(), P("head", None))
    out_specs = P(("frame", "head"), None)
    return jax.shard_map(shards, mesh=mesh, in_specs=in_specs, out_specs=out_specs, check_vma=False)
```

```python
import functools
import math

import jax
import jax.numpy as jnp
from jax import lax
from jax.experimental import pallas as pl
from jax.experimental.pallas import tpu as pltpu
from jax.sharding import PartitionSpec as P

HD = 128
TILE = 128
MAX_KEYS = 27
KEYS_PER_STEP = 3


def key_lists(tile_rows):
    seen = jnp.cumsum((tile_rows > 0).astype(jnp.int32), axis=1)
    counts = jnp.minimum(seen[:, -1], MAX_KEYS)
    slots = jnp.arange(MAX_KEYS, dtype=jnp.int32)
    lists = jnp.sum((seen[:, None, :] <= slots[None, :, None]).astype(jnp.int32), axis=2)
    last = jnp.sum((seen <= (counts - 1)[:, None]).astype(jnp.int32), axis=1)
    lists = jnp.where(slots[None, :] < counts[:, None], lists, last[:, None])
    return lists.reshape(-1), counts


def attention_kernel(lists_ref, counts_ref, q_ref, *refs, head_count, scale):
    key_refs = refs[:KEYS_PER_STEP]
    value_refs = refs[KEYS_PER_STEP : 2 * KEYS_PER_STEP]
    o_ref = refs[2 * KEYS_PER_STEP]
    top_ref, total_ref, acc_ref = refs[2 * KEYS_PER_STEP + 1 :]
    tile = pl.program_id(0)
    step = pl.program_id(1)

    @pl.when(step == 0)
    def _():
        top_ref[...] = jnp.full(top_ref.shape, -jnp.inf, jnp.float32)
        total_ref[...] = jnp.zeros(total_ref.shape, jnp.float32)
        acc_ref[...] = jnp.zeros(acc_ref.shape, jnp.float32)

    for j in range(KEYS_PER_STEP):

        @pl.when(step * KEYS_PER_STEP + j < counts_ref[tile])
        def _():
            for h in range(head_count):
                cols = pl.ds(h * HD, HD)
                q = q_ref[:, cols]
                k = key_refs[j][:, cols]
                s = lax.dot_general(
                    q, k, (((1,), (1,)), ((), ())), preferred_element_type=jnp.float32
                ) * scale
                old_top = top_ref[h]
                new_top = jnp.maximum(old_top, jnp.max(s, axis=1, keepdims=True))
                weights = jnp.exp(s - new_top)
                factor = jnp.exp(old_top - new_top)
                total_ref[h] = total_ref[h] * factor + jnp.sum(weights, axis=1, keepdims=True)
                acc_ref[h] = acc_ref[h] * factor + jnp.dot(
                    weights.astype(jnp.bfloat16),
                    value_refs[j][:, cols],
                    preferred_element_type=jnp.float32,
                )
                top_ref[h] = new_top

    @pl.when(step == pl.num_programs(1) - 1)
    def _():
        for h in range(head_count):
            o_ref[:, pl.ds(h * HD, HD)] = (acc_ref[h] / total_ref[h]).astype(o_ref.dtype)


def sparse_attention(query_vectors, pair_piece, lists, counts):
    row_count, channels = query_vectors.shape
    head_count = channels // HD
    query_tiles = row_count // TILE
    steps = MAX_KEYS // KEYS_PER_STEP

    def key_spec(j, half):
        return pl.BlockSpec(
            (TILE, channels),
            lambda i, s, lists_ref, counts_ref: (
                lists_ref[i * MAX_KEYS + s * KEYS_PER_STEP + j],
                half,
            ),
        )

    row_spec = pl.BlockSpec((TILE, channels), lambda i, s, lists_ref, counts_ref: (i, 0))
    kernel = functools.partial(
        attention_kernel, head_count=head_count, scale=1.0 / math.sqrt(HD)
    )
    return pl.pallas_call(
        kernel,
        grid_spec=pltpu.PrefetchScalarGridSpec(
            num_scalar_prefetch=2,
            grid=(query_tiles, steps),
            in_specs=[row_spec]
            + [key_spec(j, 0) for j in range(KEYS_PER_STEP)]
            + [key_spec(j, 1) for j in range(KEYS_PER_STEP)],
            out_specs=row_spec,
            scratch_shapes=[
                pltpu.VMEM((head_count, TILE, 1), jnp.float32),
                pltpu.VMEM((head_count, TILE, 1), jnp.float32),
                pltpu.VMEM((head_count, TILE, HD), jnp.float32),
            ],
        ),
        out_shape=jax.ShapeDtypeStruct((row_count, channels), jnp.bfloat16),
        compiler_params=pltpu.CompilerParams(dimension_semantics=("arbitrary", "arbitrary")),
    )(lists, counts, query_vectors, *([pair_piece] * (2 * KEYS_PER_STEP)))


def shards(query_vectors, key_vectors, value_vectors, tile_mask, out_weight):
    row_count = query_vectors.shape[0]
    frame_pos = lax.axis_index("frame")
    tiles_here = row_count // TILE
    query_tiles = lax.dynamic_slice_in_dim(tile_mask, frame_pos * tiles_here, tiles_here, 0)
    lists, counts = key_lists(query_tiles)
    pair_piece = lax.all_gather(
        jnp.concatenate([key_vectors, value_vectors], axis=1), "frame", axis=0, tiled=True
    )
    attended = sparse_attention(query_vectors, pair_piece, lists, counts)
    partial = jnp.dot(attended, out_weight, preferred_element_type=jnp.float32).astype(jnp.bfloat16)
    head_count = lax.axis_size("head")
    pieces = lax.all_to_all(
        partial.reshape(head_count, row_count // head_count, partial.shape[1]), "head", 0, 0
    )
    return jnp.sum(pieces.astype(jnp.float32), axis=0).astype(jnp.bfloat16)


def solution(mesh):
    in_specs = (P("frame", "head"), P("frame", "head"), P("frame", "head"), P(), P("head", None))
    out_specs = P(("frame", "head"), None)
    return jax.shard_map(shards, mesh=mesh, in_specs=in_specs, out_specs=out_specs, check_vma=False)
```

```python
import functools
import math

import jax
import jax.numpy as jnp
from jax import lax
from jax.experimental import pallas as pl
from jax.experimental.pallas import tpu as pltpu
from jax.sharding import PartitionSpec as P

HD = 128
TILE = 128
MAX_KEYS = 27
KEYS_PER_STEP = 9


def key_lists(tile_rows):
    seen = jnp.cumsum((tile_rows > 0).astype(jnp.int32), axis=1)
    counts = jnp.minimum(seen[:, -1], MAX_KEYS)
    slots = jnp.arange(MAX_KEYS, dtype=jnp.int32)
    lists = jnp.sum((seen[:, None, :] <= slots[None, :, None]).astype(jnp.int32), axis=2)
    last = jnp.sum((seen <= (counts - 1)[:, None]).astype(jnp.int32), axis=1)
    lists = jnp.where(slots[None, :] < counts[:, None], lists, last[:, None])
    return lists.reshape(-1), counts


def attention_kernel(lists_ref, counts_ref, q_ref, *refs, head_count, scale):
    key_refs = refs[:KEYS_PER_STEP]
    value_refs = refs[KEYS_PER_STEP : 2 * KEYS_PER_STEP]
    o_ref = refs[2 * KEYS_PER_STEP]
    top_ref, total_ref, acc_ref = refs[2 * KEYS_PER_STEP + 1 :]
    tile = pl.program_id(0)
    step = pl.program_id(1)
    valid = counts_ref[tile] - step * KEYS_PER_STEP

    @pl.when(step == 0)
    def _():
        top_ref[...] = jnp.full(top_ref.shape, -jnp.inf, jnp.float32)
        total_ref[...] = jnp.zeros(total_ref.shape, jnp.float32)
        acc_ref[...] = jnp.zeros(acc_ref.shape, jnp.float32)

    @pl.when(valid > 0)
    def _():
        column = lax.broadcasted_iota(jnp.int32, (1, KEYS_PER_STEP * TILE), 1)
        in_list = column < valid * TILE
        for h in range(head_count):
            cols = pl.ds(h * HD, HD)
            q = q_ref[:, cols]
            k = jnp.concatenate([key_refs[j][:, cols] for j in range(KEYS_PER_STEP)], axis=0)
            v = jnp.concatenate([value_refs[j][:, cols] for j in range(KEYS_PER_STEP)], axis=0)
            s = lax.dot_general(
                q, k, (((1,), (1,)), ((), ())), preferred_element_type=jnp.float32
            ) * scale
            s = jnp.where(in_list, s, -jnp.inf)
            old_top = top_ref[h]
            new_top = jnp.maximum(old_top, jnp.max(s, axis=1, keepdims=True))
            weights = jnp.exp(s - new_top)
            factor = jnp.exp(old_top - new_top)
            total_ref[h] = total_ref[h] * factor + jnp.sum(weights, axis=1, keepdims=True)
            acc_ref[h] = acc_ref[h] * factor + jnp.dot(
                weights.astype(jnp.bfloat16), v, preferred_element_type=jnp.float32
            )
            top_ref[h] = new_top

    @pl.when(step == pl.num_programs(1) - 1)
    def _():
        for h in range(head_count):
            o_ref[:, pl.ds(h * HD, HD)] = (acc_ref[h] / total_ref[h]).astype(o_ref.dtype)


def sparse_attention(query_vectors, pair_piece, lists, counts):
    row_count, channels = query_vectors.shape
    head_count = channels // HD
    query_tiles = row_count // TILE
    steps = MAX_KEYS // KEYS_PER_STEP

    def key_spec(j, half):
        return pl.BlockSpec(
            (TILE, channels),
            lambda i, s, lists_ref, counts_ref: (
                lists_ref[i * MAX_KEYS + s * KEYS_PER_STEP + j],
                half,
            ),
        )

    row_spec = pl.BlockSpec((TILE, channels), lambda i, s, lists_ref, counts_ref: (i, 0))
    kernel = functools.partial(
        attention_kernel, head_count=head_count, scale=1.0 / math.sqrt(HD)
    )
    return pl.pallas_call(
        kernel,
        grid_spec=pltpu.PrefetchScalarGridSpec(
            num_scalar_prefetch=2,
            grid=(query_tiles, steps),
            in_specs=[row_spec]
            + [key_spec(j, 0) for j in range(KEYS_PER_STEP)]
            + [key_spec(j, 1) for j in range(KEYS_PER_STEP)],
            out_specs=row_spec,
            scratch_shapes=[
                pltpu.VMEM((head_count, TILE, 1), jnp.float32),
                pltpu.VMEM((head_count, TILE, 1), jnp.float32),
                pltpu.VMEM((head_count, TILE, HD), jnp.float32),
            ],
        ),
        out_shape=jax.ShapeDtypeStruct((row_count, channels), jnp.bfloat16),
        compiler_params=pltpu.CompilerParams(dimension_semantics=("arbitrary", "arbitrary")),
    )(lists, counts, query_vectors, *([pair_piece] * (2 * KEYS_PER_STEP)))


def shards(query_vectors, key_vectors, value_vectors, tile_mask, out_weight):
    row_count = query_vectors.shape[0]
    frame_pos = lax.axis_index("frame")
    tiles_here = row_count // TILE
    query_tiles = lax.dynamic_slice_in_dim(tile_mask, frame_pos * tiles_here, tiles_here, 0)
    lists, counts = key_lists(query_tiles)
    pair_piece = lax.all_gather(
        jnp.concatenate([key_vectors, value_vectors], axis=1), "frame", axis=0, tiled=True
    )
    attended = sparse_attention(query_vectors, pair_piece, lists, counts)
    partial = jnp.dot(attended, out_weight, preferred_element_type=jnp.float32).astype(jnp.bfloat16)
    head_count = lax.axis_size("head")
    pieces = lax.all_to_all(
        partial.reshape(head_count, row_count // head_count, partial.shape[1]), "head", 0, 0
    )
    return jnp.sum(pieces.astype(jnp.float32), axis=0).astype(jnp.bfloat16)


def solution(mesh):
    in_specs = (P("frame", "head"), P("frame", "head"), P("frame", "head"), P(), P("head", None))
    out_specs = P(("frame", "head"), None)
    return jax.shard_map(shards, mesh=mesh, in_specs=in_specs, out_specs=out_specs, check_vma=False)
```

```python
import functools
import math

import jax
import jax.numpy as jnp
from jax import lax
from jax.experimental import pallas as pl
from jax.experimental.pallas import tpu as pltpu
from jax.sharding import PartitionSpec as P

HD = 128
TILE = 128
MAX_KEYS = 27
KEYS_PER_STEP = 9


def key_lists(tile_rows):
    seen = jnp.cumsum((tile_rows > 0).astype(jnp.int32), axis=1)
    counts = jnp.minimum(seen[:, -1], MAX_KEYS)
    slots = jnp.arange(MAX_KEYS, dtype=jnp.int32)
    lists = jnp.sum((seen[:, None, :] <= slots[None, :, None]).astype(jnp.int32), axis=2)
    last = jnp.sum((seen <= (counts - 1)[:, None]).astype(jnp.int32), axis=1)
    lists = jnp.where(slots[None, :] < counts[:, None], lists, last[:, None])
    return lists.reshape(-1), counts


def attention_kernel(lists_ref, counts_ref, q_ref, *refs, head_count, scale):
    key_refs = refs[:KEYS_PER_STEP]
    value_refs = refs[KEYS_PER_STEP : 2 * KEYS_PER_STEP]
    w_ref, o_ref = refs[2 * KEYS_PER_STEP : 2 * KEYS_PER_STEP + 2]
    top_ref, total_ref, acc_ref = refs[2 * KEYS_PER_STEP + 2 :]
    tile = pl.program_id(0)
    step = pl.program_id(1)
    valid = counts_ref[tile] - step * KEYS_PER_STEP

    @pl.when(step == 0)
    def _():
        top_ref[...] = jnp.full(top_ref.shape, -jnp.inf, jnp.float32)
        total_ref[...] = jnp.zeros(total_ref.shape, jnp.float32)
        acc_ref[...] = jnp.zeros(acc_ref.shape, jnp.float32)

    def update(masked):
        column = lax.broadcasted_iota(jnp.int32, (1, KEYS_PER_STEP * TILE), 1)
        in_list = column < valid * TILE
        for h in range(head_count):
            cols = pl.ds(h * HD, HD)
            q = q_ref[:, cols]
            k = jnp.concatenate([key_refs[j][:, cols] for j in range(KEYS_PER_STEP)], axis=0)
            v = jnp.concatenate([value_refs[j][:, cols] for j in range(KEYS_PER_STEP)], axis=0)
            s = lax.dot_general(
                q, k, (((1,), (1,)), ((), ())), preferred_element_type=jnp.float32
            ) * scale
            if masked:
                s = jnp.where(in_list, s, -jnp.inf)
            old_top = top_ref[h]
            new_top = jnp.maximum(old_top, jnp.max(s, axis=1, keepdims=True))
            weights = jnp.exp(s - new_top)
            factor = jnp.exp(old_top - new_top)
            total_ref[h] = total_ref[h] * factor + jnp.sum(weights, axis=1, keepdims=True)
            acc_ref[h] = acc_ref[h] * factor + jnp.dot(
                weights.astype(jnp.bfloat16), v, preferred_element_type=jnp.float32
            )
            top_ref[h] = new_top

    @pl.when(valid >= KEYS_PER_STEP)
    def _():
        update(False)

    @pl.when((valid > 0) & (valid < KEYS_PER_STEP))
    def _():
        update(True)

    @pl.when(step == pl.num_programs(1) - 1)
    def _():
        attended = jnp.concatenate(
            [(acc_ref[h] / total_ref[h]).astype(jnp.bfloat16) for h in range(head_count)], axis=1
        )
        o_ref[...] = jnp.dot(attended, w_ref[...], preferred_element_type=jnp.float32).astype(
            o_ref.dtype
        )


def sparse_attention(query_vectors, pair_piece, out_weight, lists, counts):
    row_count, channels = query_vectors.shape
    head_count = channels // HD
    query_tiles = row_count // TILE
    steps = MAX_KEYS // KEYS_PER_STEP

    def key_spec(j, half):
        return pl.BlockSpec(
            (TILE, channels),
            lambda i, s, lists_ref, counts_ref: (
                lists_ref[i * MAX_KEYS + s * KEYS_PER_STEP + j],
                half,
            ),
        )

    row_spec = pl.BlockSpec((TILE, channels), lambda i, s, lists_ref, counts_ref: (i, 0))
    kernel = functools.partial(
        attention_kernel, head_count=head_count, scale=1.0 / math.sqrt(HD)
    )
    return pl.pallas_call(
        kernel,
        grid_spec=pltpu.PrefetchScalarGridSpec(
            num_scalar_prefetch=2,
            grid=(query_tiles, steps),
            in_specs=[row_spec]
            + [key_spec(j, 0) for j in range(KEYS_PER_STEP)]
            + [key_spec(j, 1) for j in range(KEYS_PER_STEP)]
            + [pl.BlockSpec(out_weight.shape, lambda i, s, lists_ref, counts_ref: (0, 0))],
            out_specs=pl.BlockSpec(
                (TILE, out_weight.shape[1]), lambda i, s, lists_ref, counts_ref: (i, 0)
            ),
            scratch_shapes=[
                pltpu.VMEM((head_count, TILE, 1), jnp.float32),
                pltpu.VMEM((head_count, TILE, 1), jnp.float32),
                pltpu.VMEM((head_count, TILE, HD), jnp.float32),
            ],
        ),
        out_shape=jax.ShapeDtypeStruct((row_count, out_weight.shape[1]), jnp.bfloat16),
        compiler_params=pltpu.CompilerParams(dimension_semantics=("arbitrary", "arbitrary")),
    )(lists, counts, query_vectors, *([pair_piece] * (2 * KEYS_PER_STEP)), out_weight)


def shards(query_vectors, key_vectors, value_vectors, tile_mask, out_weight):
    row_count = query_vectors.shape[0]
    frame_pos = lax.axis_index("frame")
    tiles_here = row_count // TILE
    query_tiles = lax.dynamic_slice_in_dim(tile_mask, frame_pos * tiles_here, tiles_here, 0)
    lists, counts = key_lists(query_tiles)
    pair_piece = lax.all_gather(
        jnp.concatenate([key_vectors, value_vectors], axis=1), "frame", axis=0, tiled=True
    )
    partial = sparse_attention(query_vectors, pair_piece, out_weight, lists, counts)
    head_count = lax.axis_size("head")
    pieces = lax.all_to_all(
        partial.reshape(head_count, row_count // head_count, partial.shape[1]), "head", 0, 0
    )
    return jnp.sum(pieces.astype(jnp.float32), axis=0).astype(jnp.bfloat16)


def solution(mesh):
    in_specs = (P("frame", "head"), P("frame", "head"), P("frame", "head"), P(), P("head", None))
    out_specs = P(("frame", "head"), None)
    return jax.shard_map(shards, mesh=mesh, in_specs=in_specs, out_specs=out_specs, check_vma=False)
```

```python
import functools
import math

import jax
import jax.numpy as jnp
from jax import lax
from jax.experimental import pallas as pl
from jax.experimental.pallas import tpu as pltpu
from jax.sharding import PartitionSpec as P

HD = 128
TILE = 128
MAX_KEYS = 27
KEYS_PER_STEP = 9


def key_lists(tile_rows):
    seen = jnp.cumsum((tile_rows > 0).astype(jnp.int32), axis=1)
    counts = jnp.minimum(seen[:, -1], MAX_KEYS)
    slots = jnp.arange(MAX_KEYS, dtype=jnp.int32)
    lists = jnp.sum((seen[:, None, :] <= slots[None, :, None]).astype(jnp.int32), axis=2)
    last = jnp.sum((seen <= (counts - 1)[:, None]).astype(jnp.int32), axis=1)
    lists = jnp.where(slots[None, :] < counts[:, None], lists, last[:, None])
    return lists.reshape(-1), counts


def attention_kernel(lists_ref, counts_ref, q_ref, *refs, head_count, scale):
    key_refs = refs[:KEYS_PER_STEP]
    value_refs = refs[KEYS_PER_STEP : 2 * KEYS_PER_STEP]
    w_ref, o_ref = refs[2 * KEYS_PER_STEP : 2 * KEYS_PER_STEP + 2]
    top_ref, total_ref, acc_ref = refs[2 * KEYS_PER_STEP + 2 :]
    tile = pl.program_id(0)
    step = pl.program_id(1)
    valid = counts_ref[tile] - step * KEYS_PER_STEP

    @pl.when(step == 0)
    def _():
        top_ref[...] = jnp.full(top_ref.shape, -jnp.inf, jnp.float32)
        total_ref[...] = jnp.zeros(total_ref.shape, jnp.float32)
        acc_ref[...] = jnp.zeros(acc_ref.shape, jnp.float32)

    def update(masked):
        for h in range(head_count):
            cols = pl.ds(h * HD, HD)
            q = q_ref[:, cols]

            def scores(j):
                s = lax.dot_general(
                    q, key_refs[j][:, cols], (((1,), (1,)), ((), ())),
                    preferred_element_type=jnp.float32,
                ) * scale
                return s

            old_top = top_ref[h]
            new_top = old_top
            for j in range(KEYS_PER_STEP):
                row_max = jnp.max(scores(j), axis=1, keepdims=True)
                if masked:
                    row_max = jnp.where(j < valid, row_max, -jnp.inf)
                new_top = jnp.maximum(new_top, row_max)
            factor = jnp.exp(old_top - new_top)
            total = total_ref[h] * factor
            acc = acc_ref[h] * factor
            for j in range(KEYS_PER_STEP):
                weights = jnp.exp(scores(j) - new_top)
                if masked:
                    weights = jnp.where(j < valid, weights, 0.0)
                total = total + jnp.sum(weights, axis=1, keepdims=True)
                acc = acc + jnp.dot(
                    weights.astype(jnp.bfloat16), value_refs[j][:, cols],
                    preferred_element_type=jnp.float32,
                )
            total_ref[h] = total
            acc_ref[h] = acc
            top_ref[h] = new_top

    @pl.when(valid >= KEYS_PER_STEP)
    def _():
        update(False)

    @pl.when((valid > 0) & (valid < KEYS_PER_STEP))
    def _():
        update(True)

    @pl.when(step == pl.num_programs(1) - 1)
    def _():
        attended = jnp.concatenate(
            [(acc_ref[h] / total_ref[h]).astype(jnp.bfloat16) for h in range(head_count)], axis=1
        )
        o_ref[...] = jnp.dot(attended, w_ref[...], preferred_element_type=jnp.float32).astype(
            o_ref.dtype
        )


def sparse_attention(query_vectors, pair_piece, out_weight, lists, counts):
    row_count, channels = query_vectors.shape
    head_count = channels // HD
    query_tiles = row_count // TILE
    steps = MAX_KEYS // KEYS_PER_STEP

    def key_spec(j, half):
        return pl.BlockSpec(
            (TILE, channels),
            lambda i, s, lists_ref, counts_ref: (
                lists_ref[i * MAX_KEYS + s * KEYS_PER_STEP + j],
                half,
            ),
        )

    row_spec = pl.BlockSpec((TILE, channels), lambda i, s, lists_ref, counts_ref: (i, 0))
    kernel = functools.partial(
        attention_kernel, head_count=head_count, scale=1.0 / math.sqrt(HD)
    )
    return pl.pallas_call(
        kernel,
        grid_spec=pltpu.PrefetchScalarGridSpec(
            num_scalar_prefetch=2,
            grid=(query_tiles, steps),
            in_specs=[row_spec]
            + [key_spec(j, 0) for j in range(KEYS_PER_STEP)]
            + [key_spec(j, 1) for j in range(KEYS_PER_STEP)]
            + [pl.BlockSpec(out_weight.shape, lambda i, s, lists_ref, counts_ref: (0, 0))],
            out_specs=pl.BlockSpec(
                (TILE, out_weight.shape[1]), lambda i, s, lists_ref, counts_ref: (i, 0)
            ),
            scratch_shapes=[
                pltpu.VMEM((head_count, TILE, 1), jnp.float32),
                pltpu.VMEM((head_count, TILE, 1), jnp.float32),
                pltpu.VMEM((head_count, TILE, HD), jnp.float32),
            ],
        ),
        out_shape=jax.ShapeDtypeStruct((row_count, out_weight.shape[1]), jnp.bfloat16),
        compiler_params=pltpu.CompilerParams(dimension_semantics=("arbitrary", "arbitrary")),
    )(lists, counts, query_vectors, *([pair_piece] * (2 * KEYS_PER_STEP)), out_weight)


def shards(query_vectors, key_vectors, value_vectors, tile_mask, out_weight):
    row_count = query_vectors.shape[0]
    frame_pos = lax.axis_index("frame")
    tiles_here = row_count // TILE
    query_tiles = lax.dynamic_slice_in_dim(tile_mask, frame_pos * tiles_here, tiles_here, 0)
    lists, counts = key_lists(query_tiles)
    pair_piece = lax.all_gather(
        jnp.concatenate([key_vectors, value_vectors], axis=1), "frame", axis=0, tiled=True
    )
    partial = sparse_attention(query_vectors, pair_piece, out_weight, lists, counts)
    head_count = lax.axis_size("head")
    pieces = lax.all_to_all(
        partial.reshape(head_count, row_count // head_count, partial.shape[1]), "head", 0, 0
    )
    return jnp.sum(pieces.astype(jnp.float32), axis=0).astype(jnp.bfloat16)


def solution(mesh):
    in_specs = (P("frame", "head"), P("frame", "head"), P("frame", "head"), P(), P("head", None))
    out_specs = P(("frame", "head"), None)
    return jax.shard_map(shards, mesh=mesh, in_specs=in_specs, out_specs=out_specs, check_vma=False)
```

```python
import functools
import math

import jax
import jax.numpy as jnp
from jax import lax
from jax.experimental import pallas as pl
from jax.experimental.pallas import tpu as pltpu
from jax.sharding import PartitionSpec as P

HD = 128
TILE = 128
MAX_KEYS = 27
KEYS_PER_STEP = 9


def key_lists(tile_rows):
    seen = jnp.cumsum((tile_rows > 0).astype(jnp.int32), axis=1)
    counts = jnp.minimum(seen[:, -1], MAX_KEYS)
    slots = jnp.arange(MAX_KEYS, dtype=jnp.int32)
    lists = jnp.sum((seen[:, None, :] <= slots[None, :, None]).astype(jnp.int32), axis=2)
    last = jnp.sum((seen <= (counts - 1)[:, None]).astype(jnp.int32), axis=1)
    lists = jnp.where(slots[None, :] < counts[:, None], lists, last[:, None])
    return lists.reshape(-1), counts


def attention_kernel(lists_ref, counts_ref, q_ref, *refs, head_count, scale):
    pair_refs = refs[:KEYS_PER_STEP]
    w_ref, o_ref = refs[KEYS_PER_STEP : KEYS_PER_STEP + 2]
    top_ref, total_ref, acc_ref = refs[KEYS_PER_STEP + 2 :]
    channels = q_ref.shape[1]
    tile = pl.program_id(0)
    step = pl.program_id(1)
    valid = counts_ref[tile] - step * KEYS_PER_STEP

    @pl.when(step == 0)
    def _():
        top_ref[...] = jnp.full(top_ref.shape, -jnp.inf, jnp.float32)
        total_ref[...] = jnp.zeros(total_ref.shape, jnp.float32)
        acc_ref[...] = jnp.zeros(acc_ref.shape, jnp.float32)

    def update(masked):
        column = lax.broadcasted_iota(jnp.int32, (1, KEYS_PER_STEP * TILE), 1)
        in_list = column < valid * TILE
        for h in range(head_count):
            cols = pl.ds(h * HD, HD)
            q = q_ref[:, cols]
            value_cols = pl.ds(channels + h * HD, HD)
            k = jnp.concatenate([pair_refs[j][:, cols] for j in range(KEYS_PER_STEP)], axis=0)
            v = jnp.concatenate([pair_refs[j][:, value_cols] for j in range(KEYS_PER_STEP)], axis=0)
            s = lax.dot_general(
                q, k, (((1,), (1,)), ((), ())), preferred_element_type=jnp.float32
            ) * scale
            if masked:
                s = jnp.where(in_list, s, -jnp.inf)
            old_top = top_ref[h]
            new_top = jnp.maximum(old_top, jnp.max(s, axis=1, keepdims=True))
            weights = jnp.exp(s - new_top)
            factor = jnp.exp(old_top - new_top)
            total_ref[h] = total_ref[h] * factor + jnp.sum(weights, axis=1, keepdims=True)
            acc_ref[h] = acc_ref[h] * factor + jnp.dot(
                weights.astype(jnp.bfloat16), v, preferred_element_type=jnp.float32
            )
            top_ref[h] = new_top

    @pl.when(valid >= KEYS_PER_STEP)
    def _():
        update(False)

    @pl.when((valid > 0) & (valid < KEYS_PER_STEP))
    def _():
        update(True)

    @pl.when(step == pl.num_programs(1) - 1)
    def _():
        attended = jnp.concatenate(
            [(acc_ref[h] / total_ref[h]).astype(jnp.bfloat16) for h in range(head_count)], axis=1
        )
        o_ref[...] = jnp.dot(attended, w_ref[...], preferred_element_type=jnp.float32).astype(
            o_ref.dtype
        )


def sparse_attention(query_vectors, pair_piece, out_weight, lists, counts):
    row_count, channels = query_vectors.shape
    head_count = channels // HD
    query_tiles = row_count // TILE
    steps = MAX_KEYS // KEYS_PER_STEP

    def key_spec(j):
        return pl.BlockSpec(
            (TILE, 2 * channels),
            lambda i, s, lists_ref, counts_ref: (
                lists_ref[i * MAX_KEYS + s * KEYS_PER_STEP + j],
                0,
            ),
        )

    row_spec = pl.BlockSpec((TILE, channels), lambda i, s, lists_ref, counts_ref: (i, 0))
    kernel = functools.partial(
        attention_kernel, head_count=head_count, scale=1.0 / math.sqrt(HD)
    )
    return pl.pallas_call(
        kernel,
        grid_spec=pltpu.PrefetchScalarGridSpec(
            num_scalar_prefetch=2,
            grid=(query_tiles, steps),
            in_specs=[row_spec]
            + [key_spec(j) for j in range(KEYS_PER_STEP)]
            + [pl.BlockSpec(out_weight.shape, lambda i, s, lists_ref, counts_ref: (0, 0))],
            out_specs=pl.BlockSpec(
                (TILE, out_weight.shape[1]), lambda i, s, lists_ref, counts_ref: (i, 0)
            ),
            scratch_shapes=[
                pltpu.VMEM((head_count, TILE, 1), jnp.float32),
                pltpu.VMEM((head_count, TILE, 1), jnp.float32),
                pltpu.VMEM((head_count, TILE, HD), jnp.float32),
            ],
        ),
        out_shape=jax.ShapeDtypeStruct((row_count, out_weight.shape[1]), jnp.bfloat16),
        compiler_params=pltpu.CompilerParams(dimension_semantics=("arbitrary", "arbitrary")),
    )(lists, counts, query_vectors, *([pair_piece] * KEYS_PER_STEP), out_weight)


def shards(query_vectors, key_vectors, value_vectors, tile_mask, out_weight):
    row_count = query_vectors.shape[0]
    frame_pos = lax.axis_index("frame")
    tiles_here = row_count // TILE
    query_tiles = lax.dynamic_slice_in_dim(tile_mask, frame_pos * tiles_here, tiles_here, 0)
    lists, counts = key_lists(query_tiles)
    pair_piece = lax.all_gather(
        jnp.concatenate([key_vectors, value_vectors], axis=1), "frame", axis=0, tiled=True
    )
    partial = sparse_attention(query_vectors, pair_piece, out_weight, lists, counts)
    head_count = lax.axis_size("head")
    pieces = lax.all_to_all(
        partial.reshape(head_count, row_count // head_count, partial.shape[1]), "head", 0, 0
    )
    return jnp.sum(pieces.astype(jnp.float32), axis=0).astype(jnp.bfloat16)


def solution(mesh):
    in_specs = (P("frame", "head"), P("frame", "head"), P("frame", "head"), P(), P("head", None))
    out_specs = P(("frame", "head"), None)
    return jax.shard_map(shards, mesh=mesh, in_specs=in_specs, out_specs=out_specs, check_vma=False)
```

```python
import functools
import math

import jax
import jax.numpy as jnp
from jax import lax
from jax.experimental import pallas as pl
from jax.experimental.pallas import tpu as pltpu
from jax.sharding import PartitionSpec as P

HD = 128
TILE = 128
MAX_KEYS = 27
KEYS_PER_STEP = 27
CHUNK = 9


def key_lists(tile_rows):
    seen = jnp.cumsum((tile_rows > 0).astype(jnp.int32), axis=1)
    counts = jnp.minimum(seen[:, -1], MAX_KEYS)
    slots = jnp.arange(MAX_KEYS, dtype=jnp.int32)
    lists = jnp.sum((seen[:, None, :] <= slots[None, :, None]).astype(jnp.int32), axis=2)
    last = jnp.sum((seen <= (counts - 1)[:, None]).astype(jnp.int32), axis=1)
    lists = jnp.where(slots[None, :] < counts[:, None], lists, last[:, None])
    return lists.reshape(-1), counts


def attention_kernel(lists_ref, counts_ref, q_ref, *refs, head_count, scale):
    pair_refs = refs[:KEYS_PER_STEP]
    w_ref, o_ref = refs[KEYS_PER_STEP : KEYS_PER_STEP + 2]
    top_ref, total_ref, acc_ref = refs[KEYS_PER_STEP + 2 :]
    channels = q_ref.shape[1]
    tile = pl.program_id(0)
    step = pl.program_id(1)
    valid = counts_ref[tile] - step * KEYS_PER_STEP

    @pl.when(step == 0)
    def _():
        top_ref[...] = jnp.full(top_ref.shape, -jnp.inf, jnp.float32)
        total_ref[...] = jnp.zeros(total_ref.shape, jnp.float32)
        acc_ref[...] = jnp.zeros(acc_ref.shape, jnp.float32)

    def update(first, rest, masked):
        column = lax.broadcasted_iota(jnp.int32, (1, CHUNK * TILE), 1)
        in_list = column < rest * TILE
        for h in range(head_count):
            cols = pl.ds(h * HD, HD)
            value_cols = pl.ds(channels + h * HD, HD)
            q = q_ref[:, cols]
            slots = range(first, first + CHUNK)
            k = jnp.concatenate([pair_refs[j][:, cols] for j in slots], axis=0)
            v = jnp.concatenate([pair_refs[j][:, value_cols] for j in slots], axis=0)
            s = lax.dot_general(
                q, k, (((1,), (1,)), ((), ())), preferred_element_type=jnp.float32
            ) * scale
            if masked:
                s = jnp.where(in_list, s, -jnp.inf)
            old_top = top_ref[h]
            new_top = jnp.maximum(old_top, jnp.max(s, axis=1, keepdims=True))
            weights = jnp.exp(s - new_top)
            factor = jnp.exp(old_top - new_top)
            total_ref[h] = total_ref[h] * factor + jnp.sum(weights, axis=1, keepdims=True)
            acc_ref[h] = acc_ref[h] * factor + jnp.dot(
                weights.astype(jnp.bfloat16), v, preferred_element_type=jnp.float32
            )
            top_ref[h] = new_top

    for first in range(0, KEYS_PER_STEP, CHUNK):
        rest = valid - first

        @pl.when(rest >= CHUNK)
        def _():
            update(first, rest, False)

        @pl.when((rest > 0) & (rest < CHUNK))
        def _():
            update(first, rest, True)

    @pl.when(step == pl.num_programs(1) - 1)
    def _():
        attended = jnp.concatenate(
            [(acc_ref[h] / total_ref[h]).astype(jnp.bfloat16) for h in range(head_count)], axis=1
        )
        o_ref[...] = jnp.dot(attended, w_ref[...], preferred_element_type=jnp.float32).astype(
            o_ref.dtype
        )


def sparse_attention(query_vectors, pair_piece, out_weight, lists, counts):
    row_count, channels = query_vectors.shape
    head_count = channels // HD
    query_tiles = row_count // TILE
    steps = MAX_KEYS // KEYS_PER_STEP

    def key_spec(j):
        return pl.BlockSpec(
            (TILE, 2 * channels),
            lambda i, s, lists_ref, counts_ref: (
                lists_ref[i * MAX_KEYS + s * KEYS_PER_STEP + j],
                0,
            ),
        )

    row_spec = pl.BlockSpec((TILE, channels), lambda i, s, lists_ref, counts_ref: (i, 0))
    kernel = functools.partial(
        attention_kernel, head_count=head_count, scale=1.0 / math.sqrt(HD)
    )
    return pl.pallas_call(
        kernel,
        grid_spec=pltpu.PrefetchScalarGridSpec(
            num_scalar_prefetch=2,
            grid=(query_tiles, steps),
            in_specs=[row_spec]
            + [key_spec(j) for j in range(KEYS_PER_STEP)]
            + [pl.BlockSpec(out_weight.shape, lambda i, s, lists_ref, counts_ref: (0, 0))],
            out_specs=pl.BlockSpec(
                (TILE, out_weight.shape[1]), lambda i, s, lists_ref, counts_ref: (i, 0)
            ),
            scratch_shapes=[
                pltpu.VMEM((head_count, TILE, 1), jnp.float32),
                pltpu.VMEM((head_count, TILE, 1), jnp.float32),
                pltpu.VMEM((head_count, TILE, HD), jnp.float32),
            ],
        ),
        out_shape=jax.ShapeDtypeStruct((row_count, out_weight.shape[1]), jnp.bfloat16),
        compiler_params=pltpu.CompilerParams(dimension_semantics=("arbitrary", "arbitrary")),
    )(lists, counts, query_vectors, *([pair_piece] * KEYS_PER_STEP), out_weight)


def shards(query_vectors, key_vectors, value_vectors, tile_mask, out_weight):
    row_count = query_vectors.shape[0]
    frame_pos = lax.axis_index("frame")
    tiles_here = row_count // TILE
    query_tiles = lax.dynamic_slice_in_dim(tile_mask, frame_pos * tiles_here, tiles_here, 0)
    lists, counts = key_lists(query_tiles)
    pair_piece = lax.all_gather(
        jnp.concatenate([key_vectors, value_vectors], axis=1), "frame", axis=0, tiled=True
    )
    partial = sparse_attention(query_vectors, pair_piece, out_weight, lists, counts)
    head_count = lax.axis_size("head")
    pieces = lax.all_to_all(
        partial.reshape(head_count, row_count // head_count, partial.shape[1]), "head", 0, 0
    )
    return jnp.sum(pieces.astype(jnp.float32), axis=0).astype(jnp.bfloat16)


def solution(mesh):
    in_specs = (P("frame", "head"), P("frame", "head"), P("frame", "head"), P(), P("head", None))
    out_specs = P(("frame", "head"), None)
    return jax.shard_map(shards, mesh=mesh, in_specs=in_specs, out_specs=out_specs, check_vma=False)
```

```python
import functools
import math

import jax
import jax.numpy as jnp
from jax import lax
from jax.experimental import pallas as pl
from jax.experimental.pallas import tpu as pltpu
from jax.sharding import PartitionSpec as P

HD = 128
TILE = 128
MAX_KEYS = 27
KEYS_PER_STEP = 9


def key_lists(tile_rows):
    seen = jnp.cumsum((tile_rows > 0).astype(jnp.int32), axis=1)
    counts = jnp.minimum(seen[:, -1], MAX_KEYS)
    slots = jnp.arange(MAX_KEYS, dtype=jnp.int32)
    lists = jnp.sum((seen[:, None, :] <= slots[None, :, None]).astype(jnp.int32), axis=2)
    last = jnp.sum((seen <= (counts - 1)[:, None]).astype(jnp.int32), axis=1)
    lists = jnp.where(slots[None, :] < counts[:, None], lists, last[:, None])
    return lists.reshape(-1), counts


def attention_kernel(lists_ref, counts_ref, q_ref, *refs, head_count, scale):
    key_refs = refs[:KEYS_PER_STEP]
    value_refs = refs[KEYS_PER_STEP : 2 * KEYS_PER_STEP]
    w_ref, o_ref = refs[2 * KEYS_PER_STEP : 2 * KEYS_PER_STEP + 2]
    top_ref, total_ref, acc_ref = refs[2 * KEYS_PER_STEP + 2 :]
    tile = pl.program_id(0)
    step = pl.program_id(1)
    valid = counts_ref[tile] - step * KEYS_PER_STEP

    @pl.when(step == 0)
    def _():
        top_ref[...] = jnp.full(top_ref.shape, -jnp.inf, jnp.float32)
        total_ref[...] = jnp.zeros(total_ref.shape, jnp.float32)
        acc_ref[...] = jnp.zeros(acc_ref.shape, jnp.float32)

    def update(masked):
        row = lax.broadcasted_iota(jnp.int32, (KEYS_PER_STEP * TILE, 1), 0)
        in_list = row < valid * TILE
        for h in range(head_count):
            cols = pl.ds(h * HD, HD)
            q = q_ref[:, cols]
            k = jnp.concatenate([key_refs[j][:, cols] for j in range(KEYS_PER_STEP)], axis=0)
            v = jnp.concatenate([value_refs[j][:, cols] for j in range(KEYS_PER_STEP)], axis=0)
            s = lax.dot_general(
                k, q, (((1,), (1,)), ((), ())), preferred_element_type=jnp.float32
            ) * scale
            if masked:
                s = jnp.where(in_list, s, -jnp.inf)
            old_top = top_ref[h]
            new_top = jnp.maximum(old_top, jnp.max(s, axis=0, keepdims=True))
            weights = jnp.exp(s - new_top)
            factor = jnp.exp(old_top - new_top)
            total_ref[h] = total_ref[h] * factor + jnp.sum(weights, axis=0, keepdims=True)
            acc_ref[h] = acc_ref[h] * factor + lax.dot_general(
                v, weights.astype(jnp.bfloat16), (((0,), (0,)), ((), ())),
                preferred_element_type=jnp.float32,
            )
            top_ref[h] = new_top

    @pl.when(valid >= KEYS_PER_STEP)
    def _():
        update(False)

    @pl.when((valid > 0) & (valid < KEYS_PER_STEP))
    def _():
        update(True)

    @pl.when(step == pl.num_programs(1) - 1)
    def _():
        attended = jnp.concatenate(
            [(acc_ref[h] / total_ref[h]).T.astype(jnp.bfloat16) for h in range(head_count)], axis=1
        )
        o_ref[...] = jnp.dot(attended, w_ref[...], preferred_element_type=jnp.float32).astype(
            o_ref.dtype
        )


def sparse_attention(query_vectors, pair_piece, out_weight, lists, counts):
    row_count, channels = query_vectors.shape
    head_count = channels // HD
    query_tiles = row_count // TILE
    steps = MAX_KEYS // KEYS_PER_STEP

    def key_spec(j, half):
        return pl.BlockSpec(
            (TILE, channels),
            lambda i, s, lists_ref, counts_ref: (
                lists_ref[i * MAX_KEYS + s * KEYS_PER_STEP + j],
                half,
            ),
        )

    row_spec = pl.BlockSpec((TILE, channels), lambda i, s, lists_ref, counts_ref: (i, 0))
    kernel = functools.partial(
        attention_kernel, head_count=head_count, scale=1.0 / math.sqrt(HD)
    )
    return pl.pallas_call(
        kernel,
        grid_spec=pltpu.PrefetchScalarGridSpec(
            num_scalar_prefetch=2,
            grid=(query_tiles, steps),
            in_specs=[row_spec]
            + [key_spec(j, 0) for j in range(KEYS_PER_STEP)]
            + [key_spec(j, 1) for j in range(KEYS_PER_STEP)]
            + [pl.BlockSpec(out_weight.shape, lambda i, s, lists_ref, counts_ref: (0, 0))],
            out_specs=pl.BlockSpec(
                (TILE, out_weight.shape[1]), lambda i, s, lists_ref, counts_ref: (i, 0)
            ),
            scratch_shapes=[
                pltpu.VMEM((head_count, 1, TILE), jnp.float32),
                pltpu.VMEM((head_count, 1, TILE), jnp.float32),
                pltpu.VMEM((head_count, TILE, HD), jnp.float32),
            ],
        ),
        out_shape=jax.ShapeDtypeStruct((row_count, out_weight.shape[1]), jnp.bfloat16),
        compiler_params=pltpu.CompilerParams(dimension_semantics=("arbitrary", "arbitrary")),
    )(lists, counts, query_vectors, *([pair_piece] * (2 * KEYS_PER_STEP)), out_weight)


def shards(query_vectors, key_vectors, value_vectors, tile_mask, out_weight):
    row_count = query_vectors.shape[0]
    frame_pos = lax.axis_index("frame")
    tiles_here = row_count // TILE
    query_tiles = lax.dynamic_slice_in_dim(tile_mask, frame_pos * tiles_here, tiles_here, 0)
    lists, counts = key_lists(query_tiles)
    pair_piece = lax.all_gather(
        jnp.concatenate([key_vectors, value_vectors], axis=1), "frame", axis=0, tiled=True
    )
    partial = sparse_attention(query_vectors, pair_piece, out_weight, lists, counts)
    head_count = lax.axis_size("head")
    pieces = lax.all_to_all(
        partial.reshape(head_count, row_count // head_count, partial.shape[1]), "head", 0, 0
    )
    return jnp.sum(pieces.astype(jnp.float32), axis=0).astype(jnp.bfloat16)


def solution(mesh):
    in_specs = (P("frame", "head"), P("frame", "head"), P("frame", "head"), P(), P("head", None))
    out_specs = P(("frame", "head"), None)
    return jax.shard_map(shards, mesh=mesh, in_specs=in_specs, out_specs=out_specs, check_vma=False)
```

```python
import functools
import math

import jax
import jax.numpy as jnp
from jax import lax
from jax.experimental import pallas as pl
from jax.experimental.pallas import tpu as pltpu
from jax.sharding import PartitionSpec as P

HD = 128
TILE = 128
MAX_KEYS = 27
KEYS_PER_STEP = 9


def key_lists(tile_rows):
    seen = jnp.cumsum((tile_rows > 0).astype(jnp.int32), axis=1)
    counts = jnp.minimum(seen[:, -1], MAX_KEYS)
    slots = jnp.arange(MAX_KEYS, dtype=jnp.int32)
    lists = jnp.sum((seen[:, None, :] <= slots[None, :, None]).astype(jnp.int32), axis=2)
    last = jnp.sum((seen <= (counts - 1)[:, None]).astype(jnp.int32), axis=1)
    lists = jnp.where(slots[None, :] < counts[:, None], lists, last[:, None])
    return lists.reshape(-1), counts


def attention_kernel(lists_ref, counts_ref, q_ref, *refs, head_count, scale):
    pair_refs = refs[:KEYS_PER_STEP]
    w_ref, o_ref = refs[KEYS_PER_STEP : KEYS_PER_STEP + 2]
    top_ref, total_ref, acc_ref = refs[KEYS_PER_STEP + 2 :]
    channels = q_ref.shape[1]
    tile = pl.program_id(0)
    step = pl.program_id(1)
    valid = counts_ref[tile] - step * KEYS_PER_STEP

    @pl.when(step == 0)
    def _():
        top_ref[...] = jnp.full(top_ref.shape, -jnp.inf, jnp.float32)
        total_ref[...] = jnp.zeros(total_ref.shape, jnp.float32)
        acc_ref[...] = jnp.zeros(acc_ref.shape, jnp.float32)

    def update(masked):
        row = lax.broadcasted_iota(jnp.int32, (KEYS_PER_STEP * TILE, 1), 0)
        in_list = row < valid * TILE
        for h in range(head_count):
            cols = pl.ds(h * HD, HD)
            q = q_ref[:, cols]
            value_cols = pl.ds(channels + h * HD, HD)
            k = jnp.concatenate([pair_refs[j][:, cols] for j in range(KEYS_PER_STEP)], axis=0)
            v = jnp.concatenate([pair_refs[j][:, value_cols] for j in range(KEYS_PER_STEP)], axis=0)
            s = lax.dot_general(
                k, q, (((1,), (1,)), ((), ())), preferred_element_type=jnp.float32
            ) * scale
            if masked:
                s = jnp.where(in_list, s, -jnp.inf)
            old_top = top_ref[h]
            new_top = jnp.maximum(old_top, jnp.max(s, axis=0, keepdims=True))
            weights = jnp.exp(s - new_top)
            factor = jnp.exp(old_top - new_top)
            total_ref[h] = total_ref[h] * factor + jnp.sum(weights, axis=0, keepdims=True)
            acc_ref[h] = acc_ref[h] * factor + lax.dot_general(
                v, weights.astype(jnp.bfloat16), (((0,), (0,)), ((), ())),
                preferred_element_type=jnp.float32,
            )
            top_ref[h] = new_top

    @pl.when(valid >= KEYS_PER_STEP)
    def _():
        update(False)

    @pl.when((valid > 0) & (valid < KEYS_PER_STEP))
    def _():
        update(True)

    @pl.when(step == pl.num_programs(1) - 1)
    def _():
        attended = jnp.concatenate(
            [(acc_ref[h] / total_ref[h]).T.astype(jnp.bfloat16) for h in range(head_count)], axis=1
        )
        o_ref[...] = jnp.dot(attended, w_ref[...], preferred_element_type=jnp.float32).astype(
            o_ref.dtype
        )


def sparse_attention(query_vectors, pair_piece, out_weight, lists, counts):
    row_count, channels = query_vectors.shape
    head_count = channels // HD
    query_tiles = row_count // TILE
    steps = MAX_KEYS // KEYS_PER_STEP

    def key_spec(j):
        return pl.BlockSpec(
            (TILE, 2 * channels),
            lambda i, s, lists_ref, counts_ref: (
                lists_ref[i * MAX_KEYS + s * KEYS_PER_STEP + j],
                0,
            ),
        )

    row_spec = pl.BlockSpec((TILE, channels), lambda i, s, lists_ref, counts_ref: (i, 0))
    kernel = functools.partial(
        attention_kernel, head_count=head_count, scale=1.0 / math.sqrt(HD)
    )
    return pl.pallas_call(
        kernel,
        grid_spec=pltpu.PrefetchScalarGridSpec(
            num_scalar_prefetch=2,
            grid=(query_tiles, steps),
            in_specs=[row_spec]
            + [key_spec(j) for j in range(KEYS_PER_STEP)]
            + [pl.BlockSpec(out_weight.shape, lambda i, s, lists_ref, counts_ref: (0, 0))],
            out_specs=pl.BlockSpec(
                (TILE, out_weight.shape[1]), lambda i, s, lists_ref, counts_ref: (i, 0)
            ),
            scratch_shapes=[
                pltpu.VMEM((head_count, 1, TILE), jnp.float32),
                pltpu.VMEM((head_count, 1, TILE), jnp.float32),
                pltpu.VMEM((head_count, TILE, HD), jnp.float32),
            ],
        ),
        out_shape=jax.ShapeDtypeStruct((row_count, out_weight.shape[1]), jnp.bfloat16),
        compiler_params=pltpu.CompilerParams(dimension_semantics=("arbitrary", "arbitrary")),
    )(lists, counts, query_vectors, *([pair_piece] * KEYS_PER_STEP), out_weight)


def shards(query_vectors, key_vectors, value_vectors, tile_mask, out_weight):
    row_count = query_vectors.shape[0]
    frame_pos = lax.axis_index("frame")
    tiles_here = row_count // TILE
    query_tiles = lax.dynamic_slice_in_dim(tile_mask, frame_pos * tiles_here, tiles_here, 0)
    lists, counts = key_lists(query_tiles)
    pair_piece = lax.all_gather(
        jnp.concatenate([key_vectors, value_vectors], axis=1), "frame", axis=0, tiled=True
    )
    partial = sparse_attention(query_vectors, pair_piece, out_weight, lists, counts)
    head_count = lax.axis_size("head")
    pieces = lax.all_to_all(
        partial.reshape(head_count, row_count // head_count, partial.shape[1]), "head", 0, 0
    )
    return jnp.sum(pieces.astype(jnp.float32), axis=0).astype(jnp.bfloat16)


def solution(mesh):
    in_specs = (P("frame", "head"), P("frame", "head"), P("frame", "head"), P(), P("head", None))
    out_specs = P(("frame", "head"), None)
    return jax.shard_map(shards, mesh=mesh, in_specs=in_specs, out_specs=out_specs, check_vma=False)
```

```python
import functools
import math

import jax
import jax.numpy as jnp
from jax import lax
from jax.experimental import pallas as pl
from jax.experimental.pallas import tpu as pltpu
from jax.sharding import PartitionSpec as P

HD = 128
TILE = 128
MAX_KEYS = 27
KEYS_PER_STEP = 18
SLOTS = 36


def key_lists(tile_rows):
    seen = jnp.cumsum((tile_rows > 0).astype(jnp.int32), axis=1)
    counts = jnp.minimum(seen[:, -1], MAX_KEYS)
    slots = jnp.arange(SLOTS, dtype=jnp.int32)
    lists = jnp.sum((seen[:, None, :] <= slots[None, :, None]).astype(jnp.int32), axis=2)
    last = jnp.sum((seen <= (counts - 1)[:, None]).astype(jnp.int32), axis=1)
    lists = jnp.where(slots[None, :] < counts[:, None], lists, last[:, None])
    return lists.reshape(-1), counts


def attention_kernel(lists_ref, counts_ref, q_ref, *refs, head_count, scale):
    pair_refs = refs[:KEYS_PER_STEP]
    w_ref, o_ref = refs[KEYS_PER_STEP : KEYS_PER_STEP + 2]
    top_ref, total_ref, acc_ref = refs[KEYS_PER_STEP + 2 :]
    channels = q_ref.shape[1]
    tile = pl.program_id(0)
    step = pl.program_id(1)
    valid = counts_ref[tile] - step * KEYS_PER_STEP

    @pl.when(step == 0)
    def _():
        top_ref[...] = jnp.full(top_ref.shape, -jnp.inf, jnp.float32)
        total_ref[...] = jnp.zeros(total_ref.shape, jnp.float32)
        acc_ref[...] = jnp.zeros(acc_ref.shape, jnp.float32)

    def update(masked):
        row = lax.broadcasted_iota(jnp.int32, (KEYS_PER_STEP * TILE, 1), 0)
        in_list = row < valid * TILE
        for h in range(head_count):
            cols = pl.ds(h * HD, HD)
            q = q_ref[:, cols]
            value_cols = pl.ds(channels + h * HD, HD)
            k = jnp.concatenate([pair_refs[j][:, cols] for j in range(KEYS_PER_STEP)], axis=0)
            v = jnp.concatenate([pair_refs[j][:, value_cols] for j in range(KEYS_PER_STEP)], axis=0)
            s = lax.dot_general(
                k, q, (((1,), (1,)), ((), ())), preferred_element_type=jnp.float32
            ) * scale
            if masked:
                s = jnp.where(in_list, s, -jnp.inf)
            old_top = top_ref[h]
            new_top = jnp.maximum(old_top, jnp.max(s, axis=0, keepdims=True))
            weights = jnp.exp(s - new_top)
            factor = jnp.exp(old_top - new_top)
            total_ref[h] = total_ref[h] * factor + jnp.sum(weights, axis=0, keepdims=True)
            acc_ref[h] = acc_ref[h] * factor + lax.dot_general(
                v, weights.astype(jnp.bfloat16), (((0,), (0,)), ((), ())),
                preferred_element_type=jnp.float32,
            )
            top_ref[h] = new_top

    @pl.when(valid >= KEYS_PER_STEP)
    def _():
        update(False)

    @pl.when((valid > 0) & (valid < KEYS_PER_STEP))
    def _():
        update(True)

    @pl.when(step == pl.num_programs(1) - 1)
    def _():
        attended = jnp.concatenate(
            [(acc_ref[h] / total_ref[h]).T.astype(jnp.bfloat16) for h in range(head_count)], axis=1
        )
        o_ref[...] = jnp.dot(attended, w_ref[...], preferred_element_type=jnp.float32).astype(
            o_ref.dtype
        )


def sparse_attention(query_vectors, pair_piece, out_weight, lists, counts):
    row_count, channels = query_vectors.shape
    head_count = channels // HD
    query_tiles = row_count // TILE
    steps = SLOTS // KEYS_PER_STEP

    def key_spec(j):
        return pl.BlockSpec(
            (TILE, 2 * channels),
            lambda i, s, lists_ref, counts_ref: (
                lists_ref[i * SLOTS + s * KEYS_PER_STEP + j],
                0,
            ),
        )

    row_spec = pl.BlockSpec((TILE, channels), lambda i, s, lists_ref, counts_ref: (i, 0))
    kernel = functools.partial(
        attention_kernel, head_count=head_count, scale=1.0 / math.sqrt(HD)
    )
    return pl.pallas_call(
        kernel,
        grid_spec=pltpu.PrefetchScalarGridSpec(
            num_scalar_prefetch=2,
            grid=(query_tiles, steps),
            in_specs=[row_spec]
            + [key_spec(j) for j in range(KEYS_PER_STEP)]
            + [pl.BlockSpec(out_weight.shape, lambda i, s, lists_ref, counts_ref: (0, 0))],
            out_specs=pl.BlockSpec(
                (TILE, out_weight.shape[1]), lambda i, s, lists_ref, counts_ref: (i, 0)
            ),
            scratch_shapes=[
                pltpu.VMEM((head_count, 1, TILE), jnp.float32),
                pltpu.VMEM((head_count, 1, TILE), jnp.float32),
                pltpu.VMEM((head_count, TILE, HD), jnp.float32),
            ],
        ),
        out_shape=jax.ShapeDtypeStruct((row_count, out_weight.shape[1]), jnp.bfloat16),
        compiler_params=pltpu.CompilerParams(dimension_semantics=("arbitrary", "arbitrary")),
    )(lists, counts, query_vectors, *([pair_piece] * KEYS_PER_STEP), out_weight)


def shards(query_vectors, key_vectors, value_vectors, tile_mask, out_weight):
    row_count = query_vectors.shape[0]
    frame_pos = lax.axis_index("frame")
    tiles_here = row_count // TILE
    query_tiles = lax.dynamic_slice_in_dim(tile_mask, frame_pos * tiles_here, tiles_here, 0)
    lists, counts = key_lists(query_tiles)
    pair_piece = lax.all_gather(
        jnp.concatenate([key_vectors, value_vectors], axis=1), "frame", axis=0, tiled=True
    )
    partial = sparse_attention(query_vectors, pair_piece, out_weight, lists, counts)
    head_count = lax.axis_size("head")
    pieces = lax.all_to_all(
        partial.reshape(head_count, row_count // head_count, partial.shape[1]), "head", 0, 0
    )
    return jnp.sum(pieces.astype(jnp.float32), axis=0).astype(jnp.bfloat16)


def solution(mesh):
    in_specs = (P("frame", "head"), P("frame", "head"), P("frame", "head"), P(), P("head", None))
    out_specs = P(("frame", "head"), None)
    return jax.shard_map(shards, mesh=mesh, in_specs=in_specs, out_specs=out_specs, check_vma=False)
```

```python
import functools
import math

import jax
import jax.numpy as jnp
from jax import lax
from jax.experimental import pallas as pl
from jax.experimental.pallas import tpu as pltpu
from jax.sharding import PartitionSpec as P

HD = 128
TILE = 128
MAX_KEYS = 27
KEYS_PER_STEP = 6
SLOTS = 30


def key_lists(tile_rows):
    seen = jnp.cumsum((tile_rows > 0).astype(jnp.int32), axis=1)
    counts = jnp.minimum(seen[:, -1], MAX_KEYS)
    slots = jnp.arange(SLOTS, dtype=jnp.int32)
    lists = jnp.sum((seen[:, None, :] <= slots[None, :, None]).astype(jnp.int32), axis=2)
    last = jnp.sum((seen <= (counts - 1)[:, None]).astype(jnp.int32), axis=1)
    lists = jnp.where(slots[None, :] < counts[:, None], lists, last[:, None])
    return lists.reshape(-1), counts


def attention_kernel(lists_ref, counts_ref, q_ref, *refs, head_count, scale):
    pair_refs = refs[:KEYS_PER_STEP]
    w_ref, o_ref = refs[KEYS_PER_STEP : KEYS_PER_STEP + 2]
    top_ref, total_ref, acc_ref = refs[KEYS_PER_STEP + 2 :]
    channels = q_ref.shape[1]
    tile = pl.program_id(0)
    step = pl.program_id(1)
    valid = counts_ref[tile] - step * KEYS_PER_STEP

    @pl.when(step == 0)
    def _():
        top_ref[...] = jnp.full(top_ref.shape, -jnp.inf, jnp.float32)
        total_ref[...] = jnp.zeros(total_ref.shape, jnp.float32)
        acc_ref[...] = jnp.zeros(acc_ref.shape, jnp.float32)

    def update(masked):
        row = lax.broadcasted_iota(jnp.int32, (KEYS_PER_STEP * TILE, 1), 0)
        in_list = row < valid * TILE
        for h in range(head_count):
            cols = pl.ds(h * HD, HD)
            q = q_ref[:, cols]
            value_cols = pl.ds(channels + h * HD, HD)
            k = jnp.concatenate([pair_refs[j][:, cols] for j in range(KEYS_PER_STEP)], axis=0)
            v = jnp.concatenate([pair_refs[j][:, value_cols] for j in range(KEYS_PER_STEP)], axis=0)
            s = lax.dot_general(
                k, q, (((1,), (1,)), ((), ())), preferred_element_type=jnp.float32
            ) * scale
            if masked:
                s = jnp.where(in_list, s, -jnp.inf)
            old_top = top_ref[h]
            new_top = jnp.maximum(old_top, jnp.max(s, axis=0, keepdims=True))
            weights = jnp.exp(s - new_top)
            factor = jnp.exp(old_top - new_top)
            total_ref[h] = total_ref[h] * factor + jnp.sum(weights, axis=0, keepdims=True)
            acc_ref[h] = acc_ref[h] * factor + lax.dot_general(
                v, weights.astype(jnp.bfloat16), (((0,), (0,)), ((), ())),
                preferred_element_type=jnp.float32,
            )
            top_ref[h] = new_top

    @pl.when(valid >= KEYS_PER_STEP)
    def _():
        update(False)

    @pl.when((valid > 0) & (valid < KEYS_PER_STEP))
    def _():
        update(True)

    @pl.when(step == pl.num_programs(1) - 1)
    def _():
        attended = jnp.concatenate(
            [(acc_ref[h] / total_ref[h]).T.astype(jnp.bfloat16) for h in range(head_count)], axis=1
        )
        o_ref[...] = jnp.dot(attended, w_ref[...], preferred_element_type=jnp.float32).astype(
            o_ref.dtype
        )


def sparse_attention(query_vectors, pair_piece, out_weight, lists, counts):
    row_count, channels = query_vectors.shape
    head_count = channels // HD
    query_tiles = row_count // TILE
    steps = SLOTS // KEYS_PER_STEP

    def key_spec(j):
        return pl.BlockSpec(
            (TILE, 2 * channels),
            lambda i, s, lists_ref, counts_ref: (
                lists_ref[i * SLOTS + s * KEYS_PER_STEP + j],
                0,
            ),
        )

    row_spec = pl.BlockSpec((TILE, channels), lambda i, s, lists_ref, counts_ref: (i, 0))
    kernel = functools.partial(
        attention_kernel, head_count=head_count, scale=1.0 / math.sqrt(HD)
    )
    return pl.pallas_call(
        kernel,
        grid_spec=pltpu.PrefetchScalarGridSpec(
            num_scalar_prefetch=2,
            grid=(query_tiles, steps),
            in_specs=[row_spec]
            + [key_spec(j) for j in range(KEYS_PER_STEP)]
            + [pl.BlockSpec(out_weight.shape, lambda i, s, lists_ref, counts_ref: (0, 0))],
            out_specs=pl.BlockSpec(
                (TILE, out_weight.shape[1]), lambda i, s, lists_ref, counts_ref: (i, 0)
            ),
            scratch_shapes=[
                pltpu.VMEM((head_count, 1, TILE), jnp.float32),
                pltpu.VMEM((head_count, 1, TILE), jnp.float32),
                pltpu.VMEM((head_count, TILE, HD), jnp.float32),
            ],
        ),
        out_shape=jax.ShapeDtypeStruct((row_count, out_weight.shape[1]), jnp.bfloat16),
        compiler_params=pltpu.CompilerParams(dimension_semantics=("arbitrary", "arbitrary")),
    )(lists, counts, query_vectors, *([pair_piece] * KEYS_PER_STEP), out_weight)


def shards(query_vectors, key_vectors, value_vectors, tile_mask, out_weight):
    row_count = query_vectors.shape[0]
    frame_pos = lax.axis_index("frame")
    tiles_here = row_count // TILE
    query_tiles = lax.dynamic_slice_in_dim(tile_mask, frame_pos * tiles_here, tiles_here, 0)
    lists, counts = key_lists(query_tiles)
    pair_piece = lax.all_gather(
        jnp.concatenate([key_vectors, value_vectors], axis=1), "frame", axis=0, tiled=True
    )
    partial = sparse_attention(query_vectors, pair_piece, out_weight, lists, counts)
    head_count = lax.axis_size("head")
    pieces = lax.all_to_all(
        partial.reshape(head_count, row_count // head_count, partial.shape[1]), "head", 0, 0
    )
    return jnp.sum(pieces.astype(jnp.float32), axis=0).astype(jnp.bfloat16)


def solution(mesh):
    in_specs = (P("frame", "head"), P("frame", "head"), P("frame", "head"), P(), P("head", None))
    out_specs = P(("frame", "head"), None)
    return jax.shard_map(shards, mesh=mesh, in_specs=in_specs, out_specs=out_specs, check_vma=False)
```

```python
import functools
import math

import jax
import jax.numpy as jnp
from jax import lax
from jax.experimental import pallas as pl
from jax.experimental.pallas import tpu as pltpu
from jax.sharding import PartitionSpec as P

HD = 128
TILE = 128
MAX_KEYS = 27
KEYS_PER_STEP = 9


def key_lists(tile_rows):
    seen = jnp.cumsum((tile_rows > 0).astype(jnp.int32), axis=1)
    counts = jnp.minimum(seen[:, -1], MAX_KEYS)
    slots = jnp.arange(MAX_KEYS, dtype=jnp.int32)
    lists = jnp.sum((seen[:, None, :] <= slots[None, :, None]).astype(jnp.int32), axis=2)
    last = jnp.sum((seen <= (counts - 1)[:, None]).astype(jnp.int32), axis=1)
    lists = jnp.where(slots[None, :] < counts[:, None], lists, last[:, None])
    return lists.reshape(-1), counts


def attention_kernel(lists_ref, counts_ref, q_ref, *refs, head_count, scale):
    pair_refs = refs[:KEYS_PER_STEP]
    w_hbm, o_ref = refs[KEYS_PER_STEP : KEYS_PER_STEP + 2]
    top_ref, total_ref, acc_ref, w_ref, w_sem = refs[KEYS_PER_STEP + 2 :]
    channels = q_ref.shape[1]
    tile = pl.program_id(0)
    step = pl.program_id(1)
    valid = counts_ref[tile] - step * KEYS_PER_STEP
    weight_copy = pltpu.make_async_copy(w_hbm, w_ref, w_sem)

    @pl.when((tile == 0) & (step == 0))
    def _():
        weight_copy.start()

    @pl.when(step == 0)
    def _():
        top_ref[...] = jnp.full(top_ref.shape, -jnp.inf, jnp.float32)
        total_ref[...] = jnp.zeros(total_ref.shape, jnp.float32)
        acc_ref[...] = jnp.zeros(acc_ref.shape, jnp.float32)

    def update(masked):
        row = lax.broadcasted_iota(jnp.int32, (KEYS_PER_STEP * TILE, 1), 0)
        in_list = row < valid * TILE
        for h in range(head_count):
            cols = pl.ds(h * HD, HD)
            q = q_ref[:, cols]
            value_cols = pl.ds(channels + h * HD, HD)
            k = jnp.concatenate([pair_refs[j][:, cols] for j in range(KEYS_PER_STEP)], axis=0)
            v = jnp.concatenate([pair_refs[j][:, value_cols] for j in range(KEYS_PER_STEP)], axis=0)
            s = lax.dot_general(
                k, q, (((1,), (1,)), ((), ())), preferred_element_type=jnp.float32
            ) * scale
            if masked:
                s = jnp.where(in_list, s, -jnp.inf)
            old_top = top_ref[h]
            new_top = jnp.maximum(old_top, jnp.max(s, axis=0, keepdims=True))
            weights = jnp.exp(s - new_top)
            factor = jnp.exp(old_top - new_top)
            total_ref[h] = total_ref[h] * factor + jnp.sum(weights, axis=0, keepdims=True)
            acc_ref[h] = acc_ref[h] * factor + lax.dot_general(
                v, weights.astype(jnp.bfloat16), (((0,), (0,)), ((), ())),
                preferred_element_type=jnp.float32,
            )
            top_ref[h] = new_top

    @pl.when(valid >= KEYS_PER_STEP)
    def _():
        update(False)

    @pl.when((valid > 0) & (valid < KEYS_PER_STEP))
    def _():
        update(True)

    @pl.when((tile == 0) & (step == pl.num_programs(1) - 1))
    def _():
        weight_copy.wait()

    @pl.when(step == pl.num_programs(1) - 1)
    def _():
        attended = jnp.concatenate(
            [(acc_ref[h] / total_ref[h]).T.astype(jnp.bfloat16) for h in range(head_count)], axis=1
        )
        o_ref[...] = jnp.dot(attended, w_ref[...], preferred_element_type=jnp.float32).astype(
            o_ref.dtype
        )


def sparse_attention(query_vectors, pair_piece, out_weight, lists, counts):
    row_count, channels = query_vectors.shape
    head_count = channels // HD
    query_tiles = row_count // TILE
    steps = MAX_KEYS // KEYS_PER_STEP

    def key_spec(j):
        return pl.BlockSpec(
            (TILE, 2 * channels),
            lambda i, s, lists_ref, counts_ref: (
                lists_ref[i * MAX_KEYS + s * KEYS_PER_STEP + j],
                0,
            ),
        )

    row_spec = pl.BlockSpec((TILE, channels), lambda i, s, lists_ref, counts_ref: (i, 0))
    kernel = functools.partial(
        attention_kernel, head_count=head_count, scale=1.0 / math.sqrt(HD)
    )
    return pl.pallas_call(
        kernel,
        grid_spec=pltpu.PrefetchScalarGridSpec(
            num_scalar_prefetch=2,
            grid=(query_tiles, steps),
            in_specs=[row_spec]
            + [key_spec(j) for j in range(KEYS_PER_STEP)]
            + [pl.BlockSpec(memory_space=pl.ANY)],
            out_specs=pl.BlockSpec(
                (TILE, out_weight.shape[1]), lambda i, s, lists_ref, counts_ref: (i, 0)
            ),
            scratch_shapes=[
                pltpu.VMEM((head_count, 1, TILE), jnp.float32),
                pltpu.VMEM((head_count, 1, TILE), jnp.float32),
                pltpu.VMEM((head_count, TILE, HD), jnp.float32),
                pltpu.VMEM(out_weight.shape, out_weight.dtype),
                pltpu.SemaphoreType.DMA(()),
            ],
        ),
        out_shape=jax.ShapeDtypeStruct((row_count, out_weight.shape[1]), jnp.bfloat16),
        compiler_params=pltpu.CompilerParams(dimension_semantics=("arbitrary", "arbitrary")),
    )(lists, counts, query_vectors, *([pair_piece] * KEYS_PER_STEP), out_weight)


def shards(query_vectors, key_vectors, value_vectors, tile_mask, out_weight):
    row_count = query_vectors.shape[0]
    frame_pos = lax.axis_index("frame")
    tiles_here = row_count // TILE
    query_tiles = lax.dynamic_slice_in_dim(tile_mask, frame_pos * tiles_here, tiles_here, 0)
    lists, counts = key_lists(query_tiles)
    pair_piece = lax.all_gather(
        jnp.concatenate([key_vectors, value_vectors], axis=1), "frame", axis=0, tiled=True
    )
    partial = sparse_attention(query_vectors, pair_piece, out_weight, lists, counts)
    head_count = lax.axis_size("head")
    pieces = lax.all_to_all(
        partial.reshape(head_count, row_count // head_count, partial.shape[1]), "head", 0, 0
    )
    return jnp.sum(pieces.astype(jnp.float32), axis=0).astype(jnp.bfloat16)


def solution(mesh):
    in_specs = (P("frame", "head"), P("frame", "head"), P("frame", "head"), P(), P("head", None))
    out_specs = P(("frame", "head"), None)
    return jax.shard_map(shards, mesh=mesh, in_specs=in_specs, out_specs=out_specs, check_vma=False)
```
